128 devices in a mesh: row: 16 (over x, z_lo, core), col: 8 (over y, z_hi).
Axes of the slice: x: 4, y: 4, z: 4 (z_hi: 2, z_lo: 2; z = z_hi * 2 + z_lo), core: 2. Of those that a mesh axis runs over, the one named last changes fastest.
Arguments:
- coeffs: bfloat16 [32768, 1024], P('row', 'col'), may hold values from -6 to 6
- intersection: bfloat16 [32768, 32768], P('row', 'col'), may hold values from -0.006225586 to 0.006225586
- coeff_mask: int32 [256, 8], P('row', 'col'), may hold values 0 or 1
- intersection_mask: int32 [256, 256], P('row', 'col'), may hold values 0 or 1
Outputs:
- gradient: float32 [1024, 1024], P('row', 'col')
The draws below stay inside these ranges and needn't reach their ends.
All inputs are finite; a program needn't handle non-finite values. No bound on the sum of `coeff_mask` or of `intersection_mask` on one device may be relied on, other than what follows from the above.
Results may differ from the reference program's by a relative error of at most 0.0029.
Values may be sent and summed in bfloat16 or wider, within the bound.
No kernel may reach another device: no remote copies, remote signals or barrier semaphores. Data moves between devices by JAX's collectives and lax.ppermute only.
A program may use at most 128 MiB of HBM per device.

```python
import jax
import jax.numpy as jnp
from jax import lax

BLK = 128
ORB_BLOCKS = 8
ORDER = 32768
ORBITALS = 1024
N_ROW = 16
N_COL = 8


def touch_ends(drawn, key, low, largest):
    longest = drawn.shape.index(max(drawn.shape))
    spots = []
    for shift in (0, 1):
        where = [jax.random.randint(jax.random.fold_in(key, axis), (), 0, length) for axis, length in enumerate(drawn.shape)]
        where[longest] = (where[longest] + shift) % drawn.shape[longest]
        spots.append(tuple(where))
    return drawn.at[spots[0]].set(low).at[spots[1]].set(largest)


def shard_levels(own_key, dims, cuts, smallest, high):
    def one(position, parts):
        steps = jax.random.uniform(jax.random.fold_in(jax.random.fold_in(own_key, 6), position), (parts,), jnp.float32, smallest / len(cuts), high / len(cuts))
        return jnp.repeat(jnp.exp(steps), dims[position] // parts).reshape((-1,) + (1,) * (len(dims) - position - 1))

    level = one(*cuts[0])
    for cut in cuts[1:]:
        level = level * one(*cut)
    return level


def bell_draw(rng, extent, scale, bound, cuts=(), kind=jnp.bfloat16):
    loudness = shard_levels(rng, extent, cuts, -0.22, 0.18) if cuts else 1.0
    drawn = jax.random.normal(rng, extent, jnp.float32) * scale * loudness
    return jnp.minimum(jnp.maximum(drawn, -bound), bound).astype(kind)


def setup_inputs(seed: int = 0) -> dict:
    seeds = jax.random.split(jax.random.key(seed), 5)
    coeffs = bell_draw(seeds[0], (ORDER, ORBITALS), 1.0, 6.0, ((0, 16), (1, 8)))
    intersection = bell_draw(seeds[1], (ORDER, ORDER), 0.0009765625, 0.006225586, ((0, 16), (1, 8)))
    coeff_mask = touch_ends((jax.random.randint(seeds[2], (ORDER // BLK, ORB_BLOCKS), 0, 5) < 2).astype(jnp.int32), jax.random.fold_in(seeds[2], 1), 0, 1)
    intersection_mask = touch_ends((jax.random.randint(seeds[3], (ORDER // BLK, ORDER // BLK), 0, 5) < 2).astype(jnp.int32), jax.random.fold_in(seeds[3], 1), 0, 1)
    return {"coeffs": coeffs, "intersection": intersection, "coeff_mask": coeff_mask, "intersection_mask": intersection_mask}


def mask_blocks(data, mask):
    rows, cols = data.shape
    shaped = data.reshape(rows // BLK, BLK, cols // BLK, BLK)
    return (shaped * mask.astype(data.dtype)[:, None, :, None]).reshape(rows, cols)


def reference(coeffs, intersection, coeff_mask, intersection_mask):
    masked_c = mask_blocks(coeffs, coeff_mask).astype(jnp.float32)
    band = ORDER // N_ROW
    width = ORDER // N_COL
    slabs = intersection.reshape(N_ROW, band, ORDER)
    slab_masks = intersection_mask.reshape(N_ROW, band // BLK, ORDER // BLK)
    c_slabs = masked_c.reshape(N_ROW, band, ORBITALS)

    def accumulate(total, item):
        slab, slab_mask, c_rows = item
        masked_s = mask_blocks(slab, slab_mask).astype(jnp.float32)

        def group(inner, index):
            first = (index * width).astype(jnp.int32)
            s_part = lax.dynamic_slice_in_dim(masked_s, first, width, 1)
            c_part = lax.dynamic_slice_in_dim(masked_c, first, width, 0)
            partial_value = jnp.dot(s_part, c_part, precision=lax.Precision.HIGHEST).astype(jnp.bfloat16)
            partial_value = lax.optimization_barrier(partial_value).astype(jnp.float32)
            inner = inner + jnp.dot(c_rows.T, partial_value, precision=lax.Precision.HIGHEST)
            return inner, None

        total, unused = lax.scan(group, total, jnp.arange(N_COL, dtype=jnp.int32))
        return total, None

    start = jnp.zeros((ORBITALS, ORBITALS), jnp.float32)
    gradient, unused = lax.scan(accumulate, start, (slabs, slab_masks, c_slabs))
    return gradient
```

```python
import jax
import jax.numpy as jnp
from jax import lax
from jax.sharding import PartitionSpec as P

BLK = 128


def mask_blocks(data, mask):
    rows, cols = data.shape
    shaped = data.reshape(rows // BLK, BLK, cols // BLK, BLK)
    return (shaped * mask.astype(data.dtype)[:, None, :, None]).reshape(rows, cols)


def make_local(n_row, n_col):
    ratio = n_row // n_col

    perm = []
    for src_r in range(n_row):
        for o in range(n_col):
            g, h = divmod(src_r, ratio)
            dst_r = h * n_col + o
            perm.append((src_r * n_col + o, dst_r * n_col + g))

    def local(coeffs, intersection, coeff_mask, intersection_mask):
        masked_c = mask_blocks(coeffs, coeff_mask)
        rows, width = masked_c.shape
        own_rows = lax.all_gather(masked_c, "col", axis=1, tiled=True)
        moved = lax.ppermute(masked_c, ("row", "col"), perm)
        gathered = lax.all_gather(moved, "row", axis=0, tiled=False)
        group_c = (
            gathered.reshape(ratio, n_col, rows, width)
            .transpose(0, 2, 1, 3)
            .reshape(ratio * rows, n_col * width)
        )
        masked_s = mask_blocks(intersection, intersection_mask)
        product = jnp.dot(masked_s, group_c, preferred_element_type=jnp.float32).astype(jnp.bfloat16)
        pieces = product.reshape(rows, n_col, width).transpose(1, 0, 2)
        pieces = lax.all_to_all(pieces, "col", 0, 0, tiled=True)
        summed = jnp.sum(pieces.astype(jnp.float32), axis=0)
        high = summed.astype(jnp.bfloat16)
        low = (summed - high.astype(jnp.float32)).astype(jnp.bfloat16)
        both = jnp.concatenate([high, low], axis=1)
        partial = lax.dot_general(
            own_rows, both, (((0,), (0,)), ((), ())), preferred_element_type=jnp.float32
        )
        partial = partial[:, :width] + partial[:, width:]
        return lax.psum_scatter(partial, "row", scatter_dimension=0, tiled=True)

    return local


def solution(mesh):
    return jax.shard_map(
        make_local(mesh.shape["row"], mesh.shape["col"]),
        mesh=mesh,
        in_specs=(P("row", "col"), P("row", "col"), P("row", "col"), P("row", "col")),
        out_specs=P("row", "col"),
        check_vma=False,
    )
```

```python
import jax
import jax.numpy as jnp
from jax import lax
from jax.sharding import PartitionSpec as P

BLK = 128


def mask_blocks(data, mask):
    rows, cols = data.shape
    shaped = data.reshape(rows // BLK, BLK, cols // BLK, BLK)
    return (shaped * mask.astype(data.dtype)[:, None, :, None]).reshape(rows, cols)


def make_local(n_row, n_col):
    ratio = n_row // n_col

    perm = []
    for src_r in range(n_row):
        for o in range(n_col):
            g, h = divmod(src_r, ratio)
            dst_r = h * n_col + o
            perm.append((src_r * n_col + o, dst_r * n_col + g))

    def local(coeffs, intersection, coeff_mask, intersection_mask):
        masked_c = mask_blocks(coeffs, coeff_mask)
        rows, width = masked_c.shape
        own_rows = lax.all_gather(masked_c, "col", axis=1, tiled=True)
        moved = lax.ppermute(masked_c, ("row", "col"), perm)
        gathered = lax.all_gather(moved, "row", axis=0, tiled=False)
        group_c = gathered.reshape(ratio, n_col, rows, width)
        masked_s = mask_blocks(intersection, intersection_mask).reshape(rows, ratio, rows)
        pieces = jnp.einsum(
            "rhk,hokn->orn", masked_s, group_c, preferred_element_type=jnp.float32
        ).astype(jnp.bfloat16)
        pieces = lax.all_to_all(pieces, "col", 0, 0, tiled=True)
        summed = jnp.sum(pieces.astype(jnp.float32), axis=0)
        rounded = lax.reduce_precision(summed, exponent_bits=8, mantissa_bits=7)
        high = rounded.astype(jnp.bfloat16)
        low = (summed - rounded).astype(jnp.bfloat16)
        both = jnp.concatenate([high, low], axis=1)
        partial = lax.dot_general(
            own_rows, both, (((0,), (0,)), ((), ())), preferred_element_type=jnp.float32
        )
        partial = partial[:, :width] + partial[:, width:]
        spread = partial.reshape(n_row, -1, width)
        spread = lax.all_to_all(spread, "row", 0, 0, tiled=True)
        return jnp.sum(spread, axis=0)

    return local


def solution(mesh):
    return jax.shard_map(
        make_local(mesh.shape["row"], mesh.shape["col"]),
        mesh=mesh,
        in_specs=(P("row", "col"), P("row", "col"), P("row", "col"), P("row", "col")),
        out_specs=P("row", "col"),
        check_vma=False,
    )
```

```python
import jax
import jax.numpy as jnp
from jax import lax
from jax.sharding import PartitionSpec as P

BLK = 128


def mask_blocks(data, mask):
    rows, cols = data.shape
    shaped = data.reshape(rows // BLK, BLK, cols // BLK, BLK)
    return (shaped * mask.astype(data.dtype)[:, None, :, None]).reshape(rows, cols)


def make_local(n_row, n_col):
    ratio = n_row // n_col

    perm = []
    for src_r in range(n_row):
        for o in range(n_col):
            g, h = divmod(src_r, ratio)
            dst_r = h * n_col + o
            perm.append((src_r * n_col + o, dst_r * n_col + g))

    def rotate(x, k):
        return lax.ppermute(x, "col", [(c, (c + k) % n_col) for c in range(n_col)])

    def local(coeffs, intersection, coeff_mask, intersection_mask):
        masked_c = mask_blocks(coeffs, coeff_mask)
        rows, width = masked_c.shape
        me = lax.axis_index("col")
        moved = lax.ppermute(masked_c, ("row", "col"), perm)
        gathered = lax.all_gather(moved, "row", axis=0, tiled=False)
        own_rows_blocks = [masked_c] + [rotate(masked_c, k) for k in range(1, n_col)]
        group_c = gathered.reshape(ratio, n_col, rows, width)
        masked_s = mask_blocks(intersection, intersection_mask).reshape(rows, ratio, rows)

        def piece(o):
            block = lax.dynamic_index_in_dim(group_c, o, axis=1, keepdims=False)
            return jnp.einsum(
                "rhk,hkn->rn", masked_s, block, preferred_element_type=jnp.float32
            ).astype(jnp.bfloat16)

        summed = piece(me).astype(jnp.float32)
        for k in range(1, n_col):
            summed = summed + rotate(piece((me + k) % n_col), k).astype(jnp.float32)
        rounded = lax.reduce_precision(summed, exponent_bits=8, mantissa_bits=7)
        high = rounded.astype(jnp.bfloat16)
        low = (summed - rounded).astype(jnp.bfloat16)
        both = jnp.concatenate([high, low], axis=1)
        order = (me - jnp.arange(n_col)) % n_col
        own_rows = jnp.take(jnp.stack(own_rows_blocks), order, axis=0)
        partial = jnp.einsum("jkn,km->jnm", own_rows, both, preferred_element_type=jnp.float32)
        partial = (partial[:, :, :width] + partial[:, :, width:]).reshape(n_col * width, width)
        spread = partial.reshape(n_row, -1, width)
        spread = lax.all_to_all(spread, "row", 0, 0, tiled=True)
        return jnp.sum(spread, axis=0)

    return local


def solution(mesh):
    return jax.shard_map(
        make_local(mesh.shape["row"], mesh.shape["col"]),
        mesh=mesh,
        in_specs=(P("row", "col"), P("row", "col"), P("row", "col"), P("row", "col")),
        out_specs=P("row", "col"),
        check_vma=False,
    )
```

```python
import jax
import jax.numpy as jnp
from jax import lax
from jax.sharding import Mesh
from jax.sharding import PartitionSpec as P

BLK = 128
ROW = ("rx", "rz", "rc")
COL = ("cy", "cz")
CHIPS = ("rx", "rz")


def mask_blocks(data, mask):
    rows, cols = data.shape
    shaped = data.reshape(rows // BLK, BLK, cols // BLK, BLK)
    return (shaped * mask.astype(data.dtype)[:, None, :, None]).reshape(rows, cols)


def make_local(n_row, n_col, n_core):
    ratio = n_row // n_col
    assert ratio == n_core

    perm = []
    for src_r in range(n_row):
        for o in range(n_col):
            g, h = divmod(src_r, ratio)
            dst_r = o * ratio + h
            perm.append((src_r * n_col + o, dst_r * n_col + g))

    def local(coeffs, intersection, coeff_mask, intersection_mask):
        masked_c = mask_blocks(coeffs, coeff_mask)
        rows, width = masked_c.shape
        core = lax.axis_index("rc")
        own_rows = lax.all_gather(masked_c, COL, axis=1, tiled=True)
        moved = lax.ppermute(masked_c, ROW + COL, perm)
        mine = lax.all_gather(moved, CHIPS, axis=0, tiled=False)
        other = lax.ppermute(mine, "rc", [(0, 1), (1, 0)])
        masked_s = mask_blocks(intersection, intersection_mask)
        s_mine = lax.dynamic_slice_in_dim(masked_s, core * rows, rows, axis=1)
        s_other = lax.dynamic_slice_in_dim(masked_s, (1 - core) * rows, rows, axis=1)
        pieces = jnp.einsum("rk,okn->orn", s_mine, mine, preferred_element_type=jnp.float32)
        pieces = pieces + jnp.einsum(
            "rk,okn->orn", s_other, other, preferred_element_type=jnp.float32
        )
        pieces = lax.all_to_all(pieces.astype(jnp.bfloat16), COL, 0, 0, tiled=True)
        summed = jnp.sum(pieces.astype(jnp.float32), axis=0)
        rounded = lax.reduce_precision(summed, exponent_bits=8, mantissa_bits=7)
        high = rounded.astype(jnp.bfloat16)
        low = (summed - rounded).astype(jnp.bfloat16)
        both = jnp.concatenate([high, low], axis=1)
        partial = lax.dot_general(
            own_rows, both, (((0,), (0,)), ((), ())), preferred_element_type=jnp.float32
        )
        partial = partial[:, :width] + partial[:, width:]
        spread = partial.reshape(n_row, -1, width)
        spread = lax.all_to_all(spread, ROW, 0, 0, tiled=True)
        return jnp.sum(spread, axis=0)

    return local


def solution(mesh):
    n_row, n_col = mesh.shape["row"], mesh.shape["col"]
    n_core = 2
    n_y = 4
    fine = Mesh(
        mesh.devices.reshape(n_row // (2 * n_core), 2, n_core, n_y, n_col // n_y),
        ROW + COL,
    )
    return jax.shard_map(
        make_local(n_row, n_col, n_core),
        mesh=fine,
        in_specs=(P(ROW, COL), P(ROW, COL), P(ROW, COL), P(ROW, COL)),
        out_specs=P(ROW, COL),
        check_vma=False,
    )
```

```python
import jax
import jax.numpy as jnp
from jax import lax
from jax.sharding import PartitionSpec as P

BLK = 128


def mask_blocks(data, mask):
    rows, cols = data.shape
    shaped = data.reshape(rows // BLK, BLK, cols // BLK, BLK)
    return (shaped * mask.astype(data.dtype)[:, None, :, None]).reshape(rows, cols)


def make_local(n_row, n_col):
    ratio = n_row // n_col

    perm = []
    for src_r in range(n_row):
        for o in range(n_col):
            g, h = divmod(src_r, ratio)
            dst_r = h * n_col + o
            perm.append((src_r * n_col + o, dst_r * n_col + g))

    def local(coeffs, intersection, coeff_mask, intersection_mask):
        masked_c = mask_blocks(coeffs, coeff_mask)
        rows, width = masked_c.shape
        own_rows = lax.all_gather(masked_c, "col", axis=1, tiled=True)
        moved = lax.ppermute(masked_c, ("row", "col"), perm)
        gathered = lax.all_gather(moved, "row", axis=0, tiled=False)
        group_c = gathered.reshape(ratio, n_col, rows, width)
        masked_s = mask_blocks(intersection, intersection_mask).reshape(rows, ratio, rows)
        pieces = jnp.einsum(
            "rhk,hokn->orn", masked_s, group_c, preferred_element_type=jnp.float32
        ).astype(jnp.bfloat16)
        me = lax.axis_index("col")
        summed = lax.dynamic_index_in_dim(pieces, me, 0, keepdims=False).astype(jnp.float32)
        for k in range(1, n_col):
            out = lax.dynamic_index_in_dim(pieces, (me + k) % n_col, 0, keepdims=False)
            got = lax.ppermute(out, "col", [(c, (c + k) % n_col) for c in range(n_col)])
            summed = summed + got.astype(jnp.float32)
        rounded = lax.reduce_precision(summed, exponent_bits=8, mantissa_bits=7)
        high = rounded.astype(jnp.bfloat16)
        low = (summed - rounded).astype(jnp.bfloat16)
        both = jnp.concatenate([high, low], axis=1)
        partial = lax.dot_general(
            own_rows, both, (((0,), (0,)), ((), ())), preferred_element_type=jnp.float32
        )
        partial = partial[:, :width] + partial[:, width:]
        spread = partial.reshape(n_row, -1, width)
        spread = lax.all_to_all(spread, "row", 0, 0, tiled=True)
        return jnp.sum(spread, axis=0)

    return local


def solution(mesh):
    return jax.shard_map(
        make_local(mesh.shape["row"], mesh.shape["col"]),
        mesh=mesh,
        in_specs=(P("row", "col"), P("row", "col"), P("row", "col"), P("row", "col")),
        out_specs=P("row", "col"),
        check_vma=False,
    )
```

```python
import jax
import jax.numpy as jnp
from jax import lax
from jax.sharding import PartitionSpec as P

BLK = 128


def mask_blocks(data, mask):
    rows, cols = data.shape
    shaped = data.reshape(rows // BLK, BLK, cols // BLK, BLK)
    return (shaped * mask.astype(data.dtype)[:, None, :, None]).reshape(rows, cols)


def make_local(n_row, n_col):
    ratio = n_row // n_col
    assert ratio == 2

    perm = []
    for src_r in range(n_row):
        for o in range(n_col):
            g, h = divmod(src_r, ratio)
            dst_r = h * n_col + o
            perm.append((src_r * n_col + o, dst_r * n_col + g))

    def linear(r, c):
        return r * n_col + c

    spread_perms = []
    for k in range(n_col):
        pairs = []
        for r in range(n_row):
            for c in range(n_col):
                b = (c + k) % n_col
                pairs.append((linear(r, c), linear(ratio * b + r % ratio, r // ratio)))
        spread_perms.append(pairs)
    land_same = [(linear(ratio * b + h, j), linear(ratio * j + h, b))
                 for b in range(n_col) for h in range(ratio) for j in range(n_col)]
    land_other = [(linear(ratio * b + h, j), linear(ratio * j + 1 - h, b))
                  for b in range(n_col) for h in range(ratio) for j in range(n_col)]

    def local(coeffs, intersection, coeff_mask, intersection_mask):
        masked_c = mask_blocks(coeffs, coeff_mask)
        rows, width = masked_c.shape
        me_row = lax.axis_index("row")
        me_col = lax.axis_index("col")
        half = me_row % ratio
        moved = lax.ppermute(masked_c, ("row", "col"), perm)
        gathered = lax.all_gather(moved, "row", axis=0, tiled=False)
        group_c = gathered.reshape(ratio, n_col, rows, width)
        masked_s = mask_blocks(intersection, intersection_mask).reshape(rows, ratio, rows)
        pieces = jnp.einsum(
            "rhk,hokn->orn", masked_s, group_c, preferred_element_type=jnp.float32
        ).astype(jnp.bfloat16)
        summed = None
        for k in range(n_col):
            out = lax.dynamic_index_in_dim(pieces, (me_col + k) % n_col, 0, keepdims=False)
            got = lax.ppermute(out, ("row", "col"), spread_perms[k]).astype(jnp.float32)
            summed = got if summed is None else summed + got
        rounded = lax.reduce_precision(summed, exponent_bits=8, mantissa_bits=7)
        high = rounded.astype(jnp.bfloat16)
        low = (summed - rounded).astype(jnp.bfloat16)
        both = jnp.concatenate([high, low], axis=1)
        c_rows = lax.dynamic_index_in_dim(group_c, half, 0, keepdims=False)
        partial = jnp.einsum("okn,km->onm", c_rows, both, preferred_element_type=jnp.float32)
        partial = partial[:, :, :width] + partial[:, :, width:]
        partial = lax.all_to_all(partial, "col", 0, 0, tiled=True)
        total = jnp.sum(partial, axis=0).reshape(ratio, -1, width)
        mine = lax.dynamic_index_in_dim(total, half, 0, keepdims=False)
        theirs = lax.dynamic_index_in_dim(total, 1 - half, 0, keepdims=False)
        return (lax.ppermute(mine, ("row", "col"), land_same)
                + lax.ppermute(theirs, ("row", "col"), land_other))

    return local


def solution(mesh):
    return jax.shard_map(
        make_local(mesh.shape["row"], mesh.shape["col"]),
        mesh=mesh,
        in_specs=(P("row", "col"), P("row", "col"), P("row", "col"), P("row", "col")),
        out_specs=P("row", "col"),
        check_vma=False,
    )
```

```python
import jax
import jax.numpy as jnp
from jax import lax
from jax.sharding import PartitionSpec as P

BLK = 128


def mask_blocks(data, mask):
    rows, cols = data.shape
    shaped = data.reshape(rows // BLK, BLK, cols // BLK, BLK)
    return (shaped * mask.astype(data.dtype)[:, None, :, None]).reshape(rows, cols)


def make_local(n_row, n_col):
    ratio = n_row // n_col

    perm = []
    for src_r in range(n_row):
        for o in range(n_col):
            g, h = divmod(src_r, ratio)
            dst_r = h * n_col + o
            perm.append((src_r * n_col + o, dst_r * n_col + g))

    def local(coeffs, intersection, coeff_mask, intersection_mask):
        masked_c = mask_blocks(coeffs, coeff_mask)
        rows, width = masked_c.shape
        own_rows = lax.all_gather(masked_c, "col", axis=1, tiled=True)
        moved = lax.ppermute(masked_c, ("row", "col"), perm)
        half_rows = rows // 2
        gathered = [
            lax.all_gather(moved[j * half_rows:(j + 1) * half_rows], "row", axis=0, tiled=False)
            for j in range(2)
        ]
        masked_s = mask_blocks(intersection, intersection_mask).reshape(rows, ratio, 2, half_rows)
        pieces = None
        for j in range(2):
            group_c = gathered[j].reshape(ratio, n_col, half_rows, width)
            part = jnp.einsum(
                "rhk,hokn->orn", masked_s[:, :, j], group_c, preferred_element_type=jnp.float32
            )
            pieces = part if pieces is None else pieces + part
        pieces = pieces.astype(jnp.bfloat16)
        me = lax.axis_index("col")
        summed = lax.dynamic_index_in_dim(pieces, me, 0, keepdims=False).astype(jnp.float32)
        for k in range(1, n_col):
            out = lax.dynamic_index_in_dim(pieces, (me + k) % n_col, 0, keepdims=False)
            got = lax.ppermute(out, "col", [(c, (c + k) % n_col) for c in range(n_col)])
            summed = summed + got.astype(jnp.float32)
        rounded = lax.reduce_precision(summed, exponent_bits=8, mantissa_bits=7)
        high = rounded.astype(jnp.bfloat16)
        low = (summed - rounded).astype(jnp.bfloat16)
        both = jnp.concatenate([high, low], axis=1)
        partial = lax.dot_general(
            own_rows, both, (((0,), (0,)), ((), ())), preferred_element_type=jnp.float32
        )
        partial = partial[:, :width] + partial[:, width:]
        spread = partial.reshape(n_row, -1, width)
        spread = lax.all_to_all(spread, "row", 0, 0, tiled=True)
        return jnp.sum(spread, axis=0)

    return local


def solution(mesh):
    return jax.shard_map(
        make_local(mesh.shape["row"], mesh.shape["col"]),
        mesh=mesh,
        in_specs=(P("row", "col"), P("row", "col"), P("row", "col"), P("row", "col")),
        out_specs=P("row", "col"),
        check_vma=False,
    )
```

```python
import jax
import jax.numpy as jnp
from jax import lax
from jax.sharding import PartitionSpec as P

BLK = 128


def mask_blocks(data, mask):
    rows, cols = data.shape
    shaped = data.reshape(rows // BLK, BLK, cols // BLK, BLK)
    return (shaped * mask.astype(data.dtype)[:, None, :, None]).reshape(rows, cols)


def make_local(n_row, n_col):
    ratio = n_row // n_col

    perm = []
    for src_r in range(n_row):
        for o in range(n_col):
            g, h = divmod(src_r, ratio)
            dst_r = h * n_col + o
            perm.append((src_r * n_col + o, dst_r * n_col + g))

    def linear(r, c):
        return r * n_col + c

    own_perm = [(linear(n_col * h + c, g), linear(ratio * g + h, c))
                for h in range(ratio) for c in range(n_col) for g in range(n_col)]

    def local(coeffs, intersection, coeff_mask, intersection_mask):
        masked_c = mask_blocks(coeffs, coeff_mask)
        rows, width = masked_c.shape
        moved = lax.ppermute(masked_c, ("row", "col"), perm)
        gathered = lax.all_gather(moved, "row", axis=0, tiled=False)
        group_c = gathered.reshape(ratio, n_col, rows, width)
        masked_s = mask_blocks(intersection, intersection_mask).reshape(rows, ratio, rows)
        pieces = jnp.einsum(
            "rhk,hokn->orn", masked_s, group_c, preferred_element_type=jnp.float32
        ).astype(jnp.bfloat16)
        me = lax.axis_index("col")
        sent = lax.dynamic_index_in_dim(group_c, lax.axis_index("row") // n_col, 0, keepdims=False)
        own_rows = lax.ppermute(sent, ("row", "col"), own_perm)
        summed = lax.dynamic_index_in_dim(pieces, me, 0, keepdims=False).astype(jnp.float32)
        for k in range(1, n_col):
            out = lax.dynamic_index_in_dim(pieces, (me + k) % n_col, 0, keepdims=False)
            got = lax.ppermute(out, "col", [(c, (c + k) % n_col) for c in range(n_col)])
            summed = summed + got.astype(jnp.float32)
        rounded = lax.reduce_precision(summed, exponent_bits=8, mantissa_bits=7)
        high = rounded.astype(jnp.bfloat16)
        low = (summed - rounded).astype(jnp.bfloat16)
        both = jnp.concatenate([high, low], axis=1)
        partial = jnp.einsum("okn,km->onm", own_rows, both, preferred_element_type=jnp.float32)
        partial = (partial[:, :, :width] + partial[:, :, width:]).reshape(n_col * width, width)
        spread = partial.reshape(n_row, -1, width)
        spread = lax.all_to_all(spread, "row", 0, 0, tiled=True)
        return jnp.sum(spread, axis=0)

    return local


def solution(mesh):
    return jax.shard_map(
        make_local(mesh.shape["row"], mesh.shape["col"]),
        mesh=mesh,
        in_specs=(P("row", "col"), P("row", "col"), P("row", "col"), P("row", "col")),
        out_specs=P("row", "col"),
        check_vma=False,
    )
```

```python
import jax
import jax.numpy as jnp
from jax import lax
from jax.sharding import Mesh
from jax.sharding import PartitionSpec as P

BLK = 128
ROW = "row"
COL = ("cy", "cz")


def mask_blocks(data, mask):
    rows, cols = data.shape
    shaped = data.reshape(rows // BLK, BLK, cols // BLK, BLK)
    return (shaped * mask.astype(data.dtype)[:, None, :, None]).reshape(rows, cols)


def make_local(n_row, n_col):
    ratio = n_row // n_col

    perm = []
    for src_r in range(n_row):
        for o in range(n_col):
            g, h = divmod(src_r, ratio)
            dst_r = h * n_col + o
            perm.append((src_r * n_col + o, dst_r * n_col + g))

    def local(coeffs, intersection, coeff_mask, intersection_mask):
        masked_c = mask_blocks(coeffs, coeff_mask)
        rows, width = masked_c.shape
        own_rows = lax.all_gather(masked_c, "cy", axis=0, tiled=False)
        own_rows = lax.all_gather(own_rows, "cz", axis=0, tiled=False)
        moved = lax.ppermute(masked_c, (ROW,) + COL, perm)
        gathered = lax.all_gather(moved, "row", axis=0, tiled=False)
        group_c = gathered.reshape(ratio, n_col, rows, width)
        masked_s = mask_blocks(intersection, intersection_mask).reshape(rows, ratio, rows)
        pieces = jnp.einsum(
            "rhk,hokn->orn", masked_s, group_c, preferred_element_type=jnp.float32
        ).astype(jnp.bfloat16)
        me = lax.axis_index(COL)
        summed = lax.dynamic_index_in_dim(pieces, me, 0, keepdims=False).astype(jnp.float32)
        for k in range(1, n_col):
            out = lax.dynamic_index_in_dim(pieces, (me + k) % n_col, 0, keepdims=False)
            got = lax.ppermute(out, COL, [(c, (c + k) % n_col) for c in range(n_col)])
            summed = summed + got.astype(jnp.float32)
        rounded = lax.reduce_precision(summed, exponent_bits=8, mantissa_bits=7)
        high = rounded.astype(jnp.bfloat16)
        low = (summed - rounded).astype(jnp.bfloat16)
        both = jnp.concatenate([high, low], axis=1)
        partial = jnp.einsum("zykn,km->yznm", own_rows, both, preferred_element_type=jnp.float32)
        partial = (partial[..., :width] + partial[..., width:]).reshape(n_col * width, width)
        spread = partial.reshape(n_row, -1, width)
        spread = lax.all_to_all(spread, "row", 0, 0, tiled=True)
        return jnp.sum(spread, axis=0)

    return local


def solution(mesh):
    n_row, n_col = mesh.shape["row"], mesh.shape["col"]
    n_y = 4
    fine = Mesh(mesh.devices.reshape(n_row, n_y, n_col // n_y), (ROW,) + COL)
    return jax.shard_map(
        make_local(n_row, n_col),
        mesh=fine,
        in_specs=(P(ROW, COL), P(ROW, COL), P(ROW, COL), P(ROW, COL)),
        out_specs=P(ROW, COL),
        check_vma=False,
    )
```

```python
import jax
import jax.numpy as jnp
from jax import lax
from jax.sharding import PartitionSpec as P

BLK = 128


def mask_blocks(data, mask):
    rows, cols = data.shape
    shaped = data.reshape(rows // BLK, BLK, cols // BLK, BLK)
    return (shaped * mask.astype(data.dtype)[:, None, :, None]).reshape(rows, cols)


def make_local(n_row, n_col):
    ratio = n_row // n_col

    perm = []
    for src_r in range(n_row):
        for o in range(n_col):
            g, h = divmod(src_r, ratio)
            dst_r = o * ratio + h
            perm.append((src_r * n_col + o, dst_r * n_col + g))

    def local(coeffs, intersection, coeff_mask, intersection_mask):
        masked_c = mask_blocks(coeffs, coeff_mask)
        rows, width = masked_c.shape
        own_rows = lax.all_gather(masked_c, "col", axis=1, tiled=True)
        moved = lax.ppermute(masked_c, ("row", "col"), perm)
        gathered = lax.all_gather(moved, "row", axis=0, tiled=False)
        group_c = gathered.reshape(n_col, ratio * rows, width)
        masked_s = mask_blocks(intersection, intersection_mask)
        pieces = jnp.einsum(
            "rk,okn->orn", masked_s, group_c, preferred_element_type=jnp.float32
        ).astype(jnp.bfloat16)
        me = lax.axis_index("col")
        summed = lax.dynamic_index_in_dim(pieces, me, 0, keepdims=False).astype(jnp.float32)
        for k in range(1, n_col):
            out = lax.dynamic_index_in_dim(pieces, (me + k) % n_col, 0, keepdims=False)
            got = lax.ppermute(out, "col", [(c, (c + k) % n_col) for c in range(n_col)])
            summed = summed + got.astype(jnp.float32)
        rounded = lax.reduce_precision(summed, exponent_bits=8, mantissa_bits=7)
        high = rounded.astype(jnp.bfloat16)
        low = (summed - rounded).astype(jnp.bfloat16)
        both = jnp.concatenate([high, low], axis=1)
        partial = lax.dot_general(
            own_rows, both, (((0,), (0,)), ((), ())), preferred_element_type=jnp.float32
        )
        partial = partial[:, :width] + partial[:, width:]
        spread = partial.reshape(n_row, -1, width)
        spread = lax.all_to_all(spread, "row", 0, 0, tiled=True)
        return jnp.sum(spread, axis=0)

    return local


def solution(mesh):
    return jax.shard_map(
        make_local(mesh.shape["row"], mesh.shape["col"]),
        mesh=mesh,
        in_specs=(P("row", "col"), P("row", "col"), P("row", "col"), P("row", "col")),
        out_specs=P("row", "col"),
        check_vma=False,
    )
```

```python
import jax
import jax.numpy as jnp
from jax import lax
from jax.sharding import PartitionSpec as P

BLK = 128


def mask_blocks(data, mask):
    rows, cols = data.shape
    shaped = data.reshape(rows // BLK, BLK, cols // BLK, BLK)
    return (shaped * mask.astype(data.dtype)[:, None, :, None]).reshape(rows, cols)


def make_local(n_row, n_col):
    ratio = n_row // n_col

    perm = []
    for src_r in range(n_row):
        for o in range(n_col):
            g, h = divmod(src_r, ratio)
            dst_r = o * ratio + h
            perm.append((src_r * n_col + o, dst_r * n_col + g))

    def local(coeffs, intersection, coeff_mask, intersection_mask):
        masked_c = mask_blocks(coeffs, coeff_mask)
        rows, width = masked_c.shape
        own_rows = lax.all_gather(masked_c, "col", axis=1, tiled=True)
        moved = lax.ppermute(masked_c, ("row", "col"), perm)
        gathered = lax.all_gather(moved, "row", axis=0, tiled=False)
        group_c = gathered.reshape(n_col, ratio * rows, width)
        masked_s, moved = lax.optimization_barrier(
            (mask_blocks(intersection, intersection_mask), moved))
        pieces = jnp.einsum(
            "rk,okn->orn", masked_s, group_c, preferred_element_type=jnp.float32
        ).astype(jnp.bfloat16)
        me = lax.axis_index("col")
        summed = lax.dynamic_index_in_dim(pieces, me, 0, keepdims=False).astype(jnp.float32)
        for k in range(1, n_col):
            out = lax.dynamic_index_in_dim(pieces, (me + k) % n_col, 0, keepdims=False)
            got = lax.ppermute(out, "col", [(c, (c + k) % n_col) for c in range(n_col)])
            summed = summed + got.astype(jnp.float32)
        rounded = lax.reduce_precision(summed, exponent_bits=8, mantissa_bits=7)
        high = rounded.astype(jnp.bfloat16)
        low = (summed - rounded).astype(jnp.bfloat16)
        both = jnp.concatenate([high, low], axis=1)
        partial = lax.dot_general(
            own_rows, both, (((0,), (0,)), ((), ())), preferred_element_type=jnp.float32
        )
        partial = partial[:, :width] + partial[:, width:]
        spread = partial.reshape(n_row, -1, width)
        spread = lax.all_to_all(spread, "row", 0, 0, tiled=True)
        return jnp.sum(spread, axis=0)

    return local


def solution(mesh):
    return jax.shard_map(
        make_local(mesh.shape["row"], mesh.shape["col"]),
        mesh=mesh,
        in_specs=(P("row", "col"), P("row", "col"), P("row", "col"), P("row", "col")),
        out_specs=P("row", "col"),
        check_vma=False,
    )
```

```python
import jax
import jax.numpy as jnp
from jax import lax
from jax.sharding import PartitionSpec as P

BLK = 128


def mask_blocks(data, mask):
    rows, cols = data.shape
    shaped = data.reshape(rows // BLK, BLK, cols // BLK, BLK)
    return (shaped * mask.astype(data.dtype)[:, None, :, None]).reshape(rows, cols)


def make_local(n_row, n_col):
    ratio = n_row // n_col

    perm = []
    for src_r in range(n_row):
        for o in range(n_col):
            g, h = divmod(src_r, ratio)
            dst_r = o * ratio + h
            perm.append((src_r * n_col + o, dst_r * n_col + g))

    def local(coeffs, intersection, coeff_mask, intersection_mask):
        masked_c = mask_blocks(coeffs, coeff_mask)
        rows, width = masked_c.shape
        own_rows = lax.all_to_all(
            jnp.broadcast_to(masked_c, (n_col,) + masked_c.shape), "col", 0, 0, tiled=True)
        moved = lax.ppermute(masked_c, ("row", "col"), perm)
        gathered = lax.all_gather(moved, "row", axis=0, tiled=False)
        group_c = gathered.reshape(n_col, ratio * rows, width)
        masked_s, own_rows = lax.optimization_barrier(
            (mask_blocks(intersection, intersection_mask), own_rows))
        pieces = jnp.einsum(
            "rk,okn->orn", masked_s, group_c, preferred_element_type=jnp.float32
        ).astype(jnp.bfloat16)
        me = lax.axis_index("col")
        summed = lax.dynamic_index_in_dim(pieces, me, 0, keepdims=False).astype(jnp.float32)
        for k in range(1, n_col):
            out = lax.dynamic_index_in_dim(pieces, (me + k) % n_col, 0, keepdims=False)
            got = lax.ppermute(out, "col", [(c, (c + k) % n_col) for c in range(n_col)])
            summed = summed + got.astype(jnp.float32)
        rounded = lax.reduce_precision(summed, exponent_bits=8, mantissa_bits=7)
        high = rounded.astype(jnp.bfloat16)
        low = (summed - rounded).astype(jnp.bfloat16)
        both = jnp.concatenate([high, low], axis=1)
        partial = jnp.einsum("okn,km->onm", own_rows, both, preferred_element_type=jnp.float32)
        partial = (partial[..., :width] + partial[..., width:]).reshape(n_col * width, width)
        spread = partial.reshape(n_row, -1, width)
        spread = lax.all_to_all(spread, "row", 0, 0, tiled=True)
        return jnp.sum(spread, axis=0)

    return local


def solution(mesh):
    return jax.shard_map(
        make_local(mesh.shape["row"], mesh.shape["col"]),
        mesh=mesh,
        in_specs=(P("row", "col"), P("row", "col"), P("row", "col"), P("row", "col")),
        out_specs=P("row", "col"),
        check_vma=False,
    )
```

```python
import jax
import jax.numpy as jnp
from jax import lax
from jax.sharding import Mesh
from jax.sharding import PartitionSpec as P

BLK = 128
ROW = ("rx", "rz", "rc")


def mask_blocks(data, mask):
    rows, cols = data.shape
    shaped = data.reshape(rows // BLK, BLK, cols // BLK, BLK)
    return (shaped * mask.astype(data.dtype)[:, None, :, None]).reshape(rows, cols)


def make_local(n_row, n_col):
    ratio = n_row // n_col

    perm = []
    for src_r in range(n_row):
        for o in range(n_col):
            g, h = divmod(src_r, ratio)
            dst_r = h * n_col + o
            perm.append((src_r * n_col + o, dst_r * n_col + g))

    def local(coeffs, intersection, coeff_mask, intersection_mask):
        masked_c = mask_blocks(coeffs, coeff_mask)
        rows, width = masked_c.shape
        own_rows = lax.all_gather(masked_c, "col", axis=1, tiled=True)
        moved = lax.ppermute(masked_c, ROW + ("col",), perm)
        gathered = lax.all_gather(moved, ROW, axis=0, tiled=False)
        group_c = gathered.reshape(ratio, n_col, rows, width)
        masked_s = mask_blocks(intersection, intersection_mask).reshape(rows, ratio, rows)
        pieces = jnp.einsum(
            "rhk,hokn->orn", masked_s, group_c, preferred_element_type=jnp.float32
        ).astype(jnp.bfloat16)
        me = lax.axis_index("col")
        summed = lax.dynamic_index_in_dim(pieces, me, 0, keepdims=False).astype(jnp.float32)
        for k in range(1, n_col):
            out = lax.dynamic_index_in_dim(pieces, (me + k) % n_col, 0, keepdims=False)
            got = lax.ppermute(out, "col", [(c, (c + k) % n_col) for c in range(n_col)])
            summed = summed + got.astype(jnp.float32)
        rounded = lax.reduce_precision(summed, exponent_bits=8, mantissa_bits=7)
        high = rounded.astype(jnp.bfloat16)
        low = (summed - rounded).astype(jnp.bfloat16)
        both = jnp.concatenate([high, low], axis=1)
        partial = lax.dot_general(
            own_rows, both, (((0,), (0,)), ((), ())), preferred_element_type=jnp.float32
        )
        partial = partial[:, :width] + partial[:, width:]
        core = lax.axis_index("rc")
        spread = partial.reshape(n_row // 2, 2, -1, width)
        keep = lax.dynamic_index_in_dim(spread, core, 1, keepdims=False)
        give = lax.dynamic_index_in_dim(spread, 1 - core, 1, keepdims=False)
        keep = keep + lax.ppermute(give, "rc", [(0, 1), (1, 0)])
        keep = lax.all_to_all(keep, ("rx", "rz"), 0, 0, tiled=True)
        return jnp.sum(keep, axis=0)

    return local


def solution(mesh):
    n_row, n_col = mesh.shape["row"], mesh.shape["col"]
    fine = Mesh(mesh.devices.reshape(n_row // 4, 2, 2, n_col), ROW + ("col",))
    spec = P(ROW, "col")
    return jax.shard_map(
        make_local(n_row, n_col),
        mesh=fine,
        in_specs=(spec, spec, spec, spec),
        out_specs=spec,
        check_vma=False,
    )
```

```python
import jax
import jax.numpy as jnp
from jax import lax
from jax.sharding import Mesh
from jax.sharding import PartitionSpec as P

BLK = 128
ROW = ("rx", "rz", "rc")


def mask_blocks(data, mask):
    rows, cols = data.shape
    shaped = data.reshape(rows // BLK, BLK, cols // BLK, BLK)
    return (shaped * mask.astype(data.dtype)[:, None, :, None]).reshape(rows, cols)


def make_local(n_row, n_col):
    ratio = n_row // n_col

    perm = []
    for src_r in range(n_row):
        for o in range(n_col):
            g, h = divmod(src_r, ratio)
            dst_r = o * ratio + h
            perm.append((src_r * n_col + o, dst_r * n_col + g))

    def local(coeffs, intersection, coeff_mask, intersection_mask):
        masked_c = mask_blocks(coeffs, coeff_mask)
        rows, width = masked_c.shape
        own_rows = lax.all_gather(masked_c, "col", axis=1, tiled=True)
        moved = lax.ppermute(masked_c, ROW + ("col",), perm)
        gathered = lax.all_gather(moved, ROW, axis=0, tiled=False)
        group_c = gathered.reshape(n_col, ratio * rows, width)
        masked_s, _ = lax.optimization_barrier(
            (mask_blocks(intersection, intersection_mask), moved))
        pieces = jnp.einsum(
            "rk,okn->orn", masked_s, group_c, preferred_element_type=jnp.float32
        ).astype(jnp.bfloat16)
        me = lax.axis_index("col")
        summed = lax.dynamic_index_in_dim(pieces, me, 0, keepdims=False).astype(jnp.float32)
        for k in range(1, n_col):
            out = lax.dynamic_index_in_dim(pieces, (me + k) % n_col, 0, keepdims=False)
            got = lax.ppermute(out, "col", [(c, (c + k) % n_col) for c in range(n_col)])
            summed = summed + got.astype(jnp.float32)
        rounded = lax.reduce_precision(summed, exponent_bits=8, mantissa_bits=7)
        high = rounded.astype(jnp.bfloat16)
        low = (summed - rounded).astype(jnp.bfloat16)
        both = jnp.concatenate([high, low], axis=1)
        partial = lax.dot_general(
            own_rows, both, (((0,), (0,)), ((), ())), preferred_element_type=jnp.float32
        )
        partial = partial[:, :width] + partial[:, width:]
        core = lax.axis_index("rc")
        spread = partial.reshape(n_row // 2, 2, -1, width)
        keep = lax.dynamic_index_in_dim(spread, core, 1, keepdims=False)
        give = lax.dynamic_index_in_dim(spread, 1 - core, 1, keepdims=False)
        keep = keep + lax.ppermute(give, "rc", [(0, 1), (1, 0)])
        keep = lax.all_to_all(keep, ("rx", "rz"), 0, 0, tiled=True)
        return jnp.sum(keep, axis=0)

    return local


def solution(mesh):
    n_row, n_col = mesh.shape["row"], mesh.shape["col"]
    fine = Mesh(mesh.devices.reshape(n_row // 4, 2, 2, n_col), ROW + ("col",))
    spec = P(ROW, "col")
    return jax.shard_map(
        make_local(n_row, n_col),
        mesh=fine,
        in_specs=(spec, spec, spec, spec),
        out_specs=spec,
        check_vma=False,
    )
```
